512 devices in a mesh: ctx: 64 (over x_hi, z, core), head: 8 (over x_lo, y).
Axes of the slice: x: 4 (x_hi: 2, x_lo: 2; x = x_hi * 2 + x_lo), y: 4, z: 16, core: 2. Of those that a mesh axis runs over, the one named last changes fastest.
Arguments:
- q_latent: bfloat16 [8192, 64, 512], P('ctx', 'head'), may hold values from -1.25 to 1.25
- q_rope: bfloat16 [8192, 4096], P('ctx', 'head'), may hold values from -1.25 to 1.25
- attn_out: bfloat16 [8192, 64, 512], P('ctx', 'head'), may hold values from -4 to 4
- grad_out: bfloat16 [8192, 64, 512], P('ctx', 'head'), may hold values from -1 to 1
- log_total: float32 [8192, 64], P('ctx', 'head'), may hold values from 4 to 6
- latent: bfloat16 [8192, 512], P('ctx'), may hold values from -2.5 to 2.5
- key_rope: bfloat16 [8192, 64], P('ctx'), may hold values from -2.5 to 2.5
- doc_start: int32 [8192], P('ctx'), may hold values from 0 to 8191, as said below
Outputs:
- grad_q_latent: bfloat16 [8192, 64, 512], P('ctx', 'head')
- grad_q_rope: bfloat16 [8192, 4096], P('ctx', 'head')
- grad_latent: bfloat16 [8192, 512], P(('ctx', 'head'))
- grad_key_rope: bfloat16 [8192, 64], P(('ctx', 'head'))
The draws below stay inside these ranges and needn't reach their ends.
Inputs may be any that keep to these rules, and one draw needn't show every extreme that they name: doc_start[t] is the first token of the document that holds token t. Documents are runs of 1 to 897 tokens laid end to end from token 0; one document has exactly 897 tokens, and the last token of the sequence is a document of its own.
All inputs are finite; a program needn't handle non-finite values.
Results may differ from the reference program's by a relative error of at most 0.0056.
Values may be sent and summed in bfloat16 or wider, within the bound.
No kernel may reach another device: no remote copies, remote signals or barrier semaphores. Data moves between devices by JAX's collectives and lax.ppermute only.
A program may use at most 64 MiB of HBM per device.

```python
import jax
import jax.numpy as jnp
from jax import lax

LAT = 512
ROPE = 64
NOPE = 128
HEADS = 64
TOK_DEV = 128
LEVELS = 3
DOC_MAX = 897
TOKENS = 8192
N_CTX = 64


def draw_doc_start(key, part):
    base_key = jax.random.fold_in(key, 11)
    key_len, key_long = jax.random.split(base_key)
    lengths = jax.random.randint(key_len, (TOKENS,), 1, DOC_MAX + 1, dtype=jnp.int32)
    long_index = jax.random.randint(key_long, (), 0, TOKENS // DOC_MAX - 1, dtype=jnp.int32)
    lengths = jnp.where(jnp.arange(TOKENS, dtype=jnp.int32) == long_index, DOC_MAX, lengths)
    doc_ends = jnp.cumsum(lengths).astype(jnp.int32)
    positions = jnp.arange(TOKENS, dtype=jnp.int32)
    doc_index = jnp.searchsorted(doc_ends, positions, side='right')
    doc_starts = (doc_ends - lengths)[doc_index]
    doc_starts = jnp.where(positions == TOKENS - 1, TOKENS - 1, doc_starts)
    return doc_starts.astype(jnp.int32)


def steps_of(rng, shape, shards, low, top_value):
    loudness = 1.0
    for dim, blocks in shards:
        draws = jax.random.uniform(jax.random.fold_in(jax.random.fold_in(rng, 6), dim), (blocks,), jnp.float32, low / len(shards), top_value / len(shards))
        loudness = loudness * jnp.repeat(jnp.exp(draws), shape[dim] // blocks).reshape((-1,) + (1,) * (len(shape) - 1 - dim))
    return loudness


def scatter_about(own_key, extent, deviation, reach, cuts=(), kind=jnp.bfloat16):
    gain = steps_of(own_key, extent, cuts, -0.22, 0.18) if cuts else 1.0
    result = jax.random.normal(own_key, extent, jnp.float32) * deviation * gain
    return jnp.minimum(jnp.maximum(result, -reach), reach).astype(kind)


def setup_inputs(seed: int = 0) -> dict:
    seeds = jax.random.split(jax.random.key(seed), 9)
    return {
        "q_latent": scatter_about(seeds[0], (TOKENS, HEADS, LAT), 0.5, 1.25, ((0, 64), (1, 8))),
        "q_rope": scatter_about(seeds[1], (TOKENS, HEADS * ROPE), 0.5, 1.25, ((0, 64), (1, 8))),
        "attn_out": scatter_about(seeds[2], (TOKENS, HEADS, LAT), 1.0, 4.0, ((0, 64), (1, 8))),
        "grad_out": scatter_about(seeds[3], (TOKENS, HEADS, LAT), 0.2, 1.0, ((0, 64), (1, 8))),
        "log_total": jnp.clip(4.0 + 2.0 * jax.random.uniform(seeds[4], (TOKENS, HEADS), jnp.float32) ** steps_of(seeds[4], (TOKENS, HEADS), ((0, 64), (1, 8)), -0.2, 0.2), 4.0, 6.0),
        "latent": scatter_about(seeds[5], (TOKENS, LAT), 1.0, 2.5, ((0, 64),)),
        "key_rope": scatter_about(seeds[6], (TOKENS, ROPE), 1.0, 2.5, ((0, 64),)),
        "doc_start": draw_doc_start(jax.random.fold_in(seeds[8], 71), 0),
    }


def tile_terms(q_lat, q_rot, grad_rows, row_delta, log_rows, starts, query_pos, latent_blk, rope_blk, key_first, softmax_scale):
    key_pos = key_first + jnp.arange(latent_blk.shape[0], dtype=jnp.int32)
    visible = ((key_pos[None, :] >= starts[:, None]) & (key_pos[None, :] <= query_pos[:, None]))[:, None, :]
    q_wide = q_lat.astype(jnp.float32)
    rot_wide = q_rot.astype(jnp.float32)
    grad_wide = grad_rows.astype(jnp.float32)
    lat_wide = latent_blk.astype(jnp.float32)
    key_wide = rope_blk.astype(jnp.float32)
    scores = (jnp.einsum('thc,kc->thk', q_wide, lat_wide) + jnp.einsum('thr,kr->thk', rot_wide, key_wide)) * softmax_scale
    probs = jnp.where(visible, jnp.exp(jnp.where(visible, scores, 0.0) - log_rows[:, :, None]), 0.0)
    grad_probs = jnp.einsum('thc,kc->thk', grad_wide, lat_wide)
    grad_scores = probs * (grad_probs - row_delta[:, :, None])
    probs_b = lax.optimization_barrier(probs.astype(jnp.bfloat16)).astype(jnp.float32)
    grad_b = lax.optimization_barrier(grad_scores.astype(jnp.bfloat16)).astype(jnp.float32)
    grad_qlat = softmax_scale * jnp.einsum('thk,kc->thc', grad_b, lat_wide)
    grad_qrot = softmax_scale * jnp.einsum('thk,kr->thr', grad_b, key_wide)
    grad_lat = softmax_scale * jnp.einsum('thk,thc->kc', grad_b, q_wide) + jnp.einsum('thk,thc->kc', probs_b, grad_wide)
    grad_rot = softmax_scale * jnp.einsum('thk,thr->kr', grad_b, rot_wide)
    return grad_qlat, grad_qrot, grad_lat, grad_rot


def reference(q_latent, q_rope, attn_out, grad_out, log_total, latent, key_rope, doc_start):
    tiles = N_CTX
    span = 2 ** LEVELS
    softmax_scale = (NOPE + ROPE) ** -0.5
    q_lat = q_latent.reshape(tiles, TOK_DEV, HEADS, LAT)
    q_rot = q_rope.reshape(tiles, TOK_DEV, HEADS, ROPE)
    grad_rows = grad_out.reshape(tiles, TOK_DEV, HEADS, LAT)
    out_rows = attn_out.reshape(tiles, TOK_DEV, HEADS, LAT)
    log_rows = log_total.reshape(tiles, TOK_DEV, HEADS)
    starts = doc_start.reshape(tiles, TOK_DEV)
    pad_lat = jnp.concatenate([jnp.zeros((span - 1, TOK_DEV, LAT), latent.dtype), latent.reshape(tiles, TOK_DEV, LAT)], 0)
    pad_rot = jnp.concatenate([jnp.zeros((span - 1, TOK_DEV, ROPE), key_rope.dtype), key_rope.reshape(tiles, TOK_DEV, ROPE)], 0)

    def per_tile(tile_index):
        own_q = q_lat[tile_index]
        own_rot = q_rot[tile_index]
        own_grad = grad_rows[tile_index]
        own_log = log_rows[tile_index]
        own_starts = starts[tile_index]
        row_delta = jnp.einsum('thc,thc->th', own_grad.astype(jnp.float32), out_rows[tile_index].astype(jnp.float32))
        query_pos = tile_index * TOK_DEV + jnp.arange(TOK_DEV, dtype=jnp.int32)
        earliest = jnp.min(own_starts)

        def visit(totals, offset):
            key_tile = tile_index - (span - 1) + offset
            latent_blk = lax.dynamic_index_in_dim(pad_lat, tile_index + offset, 0, keepdims=False)
            rope_blk = lax.dynamic_index_in_dim(pad_rot, tile_index + offset, 0, keepdims=False)
            key_first = key_tile * TOK_DEV

            def compute(unused):
                return tile_terms(own_q, own_rot, own_grad, row_delta, own_log, own_starts, query_pos, latent_blk, rope_blk, key_first, softmax_scale)

            def skipped(unused):
                return (jnp.zeros((TOK_DEV, HEADS, LAT), jnp.float32), jnp.zeros((TOK_DEV, HEADS, ROPE), jnp.float32),
                        jnp.zeros((TOK_DEV, LAT), jnp.float32), jnp.zeros((TOK_DEV, ROPE), jnp.float32))

            terms = lax.cond(earliest <= key_first + TOK_DEV - 1, compute, skipped, 0)
            return (totals[0] + terms[0], totals[1] + terms[1]), (terms[2], terms[3])

        init = (jnp.zeros((TOK_DEV, HEADS, LAT), jnp.float32), jnp.zeros((TOK_DEV, HEADS, ROPE), jnp.float32))
        totals, parts = lax.scan(visit, init, jnp.arange(span, dtype=jnp.int32))
        return (totals[0].astype(jnp.bfloat16), totals[1].astype(jnp.bfloat16)), parts

    (grad_qlat, grad_qrot), (part_lat, part_rot) = lax.map(per_tile, jnp.arange(tiles, dtype=jnp.int32))
    grad_lat = jnp.zeros((tiles + span - 1, TOK_DEV, LAT), jnp.float32)
    grad_rot = jnp.zeros((tiles + span - 1, TOK_DEV, ROPE), jnp.float32)
    for offset in range(span):
        grad_lat = grad_lat.at[offset:offset + tiles].add(part_lat[:, offset])
        grad_rot = grad_rot.at[offset:offset + tiles].add(part_rot[:, offset])
    grad_lat = grad_lat[span - 1:]
    grad_rot = grad_rot[span - 1:]
    return (grad_qlat.reshape(TOKENS, HEADS, LAT),
            grad_qrot.reshape(TOKENS, HEADS * ROPE),
            grad_lat.reshape(TOKENS, LAT).astype(jnp.bfloat16),
            grad_rot.reshape(TOKENS, ROPE).astype(jnp.bfloat16))
```

```python
import jax
import jax.numpy as jnp
from jax import lax
from jax.sharding import PartitionSpec as P

ROPE = 64
NOPE = 128
LEVELS = 3


def shifted(x, axis, by):
    count = lax.axis_size(axis)
    pairs = [(i, i + by) for i in range(count) if 0 <= i + by < count]
    return lax.ppermute(x, axis, pairs)


def local(q_latent, q_rope, attn_out, grad_out, log_total, latent, key_rope, doc_start):
    tok_rows, head_count, lat_width = q_latent.shape
    rope_width = key_rope.shape[1]
    span = 2**LEVELS
    groups = lax.axis_size("head")
    softmax_scale = (NOPE + ROPE) ** (-0.5)
    q_rot = q_rope.reshape(tok_rows, head_count, rope_width)
    row_delta = jnp.einsum("thc,thc->th", grad_out, attn_out, preferred_element_type=jnp.float32)
    own_tile = lax.axis_index("ctx")
    query_pos = own_tile * tok_rows + jnp.arange(tok_rows, dtype=jnp.int32)

    keys = jnp.concatenate([latent, key_rope], axis=1)[None]
    width = 1
    while width < span:
        keys = jnp.concatenate([shifted(keys, "ctx", width), keys], axis=0)
        width *= 2
    keys = keys.reshape(span * tok_rows, lat_width + rope_width)
    lat_all = keys[:, :lat_width]
    rot_all = keys[:, lat_width:]

    key_pos = (own_tile - span + 1) * tok_rows + jnp.arange(span * tok_rows, dtype=jnp.int32)
    visible = (
        (key_pos[None, :] >= doc_start[:, None]) & (key_pos[None, :] <= query_pos[:, None])
    )[:, None, :]
    scores = (
        jnp.einsum("thc,kc->thk", q_latent, lat_all, preferred_element_type=jnp.float32)
        + jnp.einsum("thr,kr->thk", q_rot, rot_all, preferred_element_type=jnp.float32)
    ) * softmax_scale
    probs = jnp.where(
        visible, jnp.exp(jnp.where(visible, scores, 0.0) - log_total[:, :, None]), 0.0
    )
    grad_probs = jnp.einsum("thc,kc->thk", grad_out, lat_all, preferred_element_type=jnp.float32)
    grad_scores = probs * (grad_probs - row_delta[:, :, None])
    probs_b = probs.astype(jnp.bfloat16)
    grad_b = grad_scores.astype(jnp.bfloat16)
    grad_qlat = softmax_scale * jnp.einsum(
        "thk,kc->thc", grad_b, lat_all, preferred_element_type=jnp.float32
    )
    grad_qrot = softmax_scale * jnp.einsum(
        "thk,kr->thr", grad_b, rot_all, preferred_element_type=jnp.float32
    )
    grad_lat = softmax_scale * jnp.einsum(
        "thk,thc->kc", grad_b, q_latent, preferred_element_type=jnp.float32
    ) + jnp.einsum("thk,thc->kc", probs_b, grad_out, preferred_element_type=jnp.float32)
    grad_rot = softmax_scale * jnp.einsum(
        "thk,thr->kr", grad_b, q_rot, preferred_element_type=jnp.float32
    )

    part = jnp.concatenate([grad_lat, grad_rot], axis=1)
    block = tok_rows // groups
    part = part.reshape(span, groups, block, lat_width + rope_width)
    part = lax.all_to_all(part, "head", 1, 1, tiled=True).sum(axis=1)

    width = span
    while width > 1:
        half = width // 2
        part = part[half:] + shifted(part[:half], "ctx", -half)
        width = half
    owned = part[0]
    return (
        grad_qlat.astype(jnp.bfloat16),
        grad_qrot.reshape(tok_rows, head_count * rope_width).astype(jnp.bfloat16),
        owned[:, :lat_width].astype(jnp.bfloat16),
        owned[:, lat_width:].astype(jnp.bfloat16),
    )


def solution(mesh):
    in_specs = (
        P("ctx", "head", None),
        P("ctx", "head"),
        P("ctx", "head", None),
        P("ctx", "head", None),
        P("ctx", "head"),
        P("ctx", None),
        P("ctx", None),
        P("ctx"),
    )
    out_specs = (
        P("ctx", "head", None),
        P("ctx", "head"),
        P(("ctx", "head"), None),
        P(("ctx", "head"), None),
    )
    return jax.shard_map(local, mesh=mesh, in_specs=in_specs, out_specs=out_specs, check_vma=False)
```

```python
import jax
import jax.numpy as jnp
from jax import lax
from jax.sharding import PartitionSpec as P

ROPE = 64
NOPE = 128
LEVELS = 3


def shifted(x, axis, by):
    count = lax.axis_size(axis)
    pairs = [(i, i + by) for i in range(count) if 0 <= i + by < count]
    return lax.ppermute(x, axis, pairs)


def window_terms(q_latent, q_rot, grad_out, row_delta, log_total, doc_start, query_pos, keys, key_first):
    lat_width = q_latent.shape[2]
    softmax_scale = (NOPE + ROPE) ** (-0.5)
    lat_all = keys[:, :lat_width]
    rot_all = keys[:, lat_width:]
    key_pos = key_first + jnp.arange(keys.shape[0], dtype=jnp.int32)
    visible = (
        (key_pos[None, :] >= doc_start[:, None]) & (key_pos[None, :] <= query_pos[:, None])
    )[:, None, :]
    scores = (
        jnp.einsum("thc,kc->thk", q_latent, lat_all, preferred_element_type=jnp.float32)
        + jnp.einsum("thr,kr->thk", q_rot, rot_all, preferred_element_type=jnp.float32)
    ) * softmax_scale
    probs = jnp.where(
        visible, jnp.exp(jnp.where(visible, scores, 0.0) - log_total[:, :, None]), 0.0
    )
    grad_probs = jnp.einsum("thc,kc->thk", grad_out, lat_all, preferred_element_type=jnp.float32)
    grad_scores = probs * (grad_probs - row_delta[:, :, None])
    probs_b = probs.astype(jnp.bfloat16)
    grad_b = grad_scores.astype(jnp.bfloat16)
    grad_qlat = jnp.einsum("thk,kc->thc", grad_b, lat_all, preferred_element_type=jnp.float32)
    grad_qrot = jnp.einsum("thk,kr->thr", grad_b, rot_all, preferred_element_type=jnp.float32)
    grad_lat = softmax_scale * jnp.einsum(
        "thk,thc->kc", grad_b, q_latent, preferred_element_type=jnp.float32
    ) + jnp.einsum("thk,thc->kc", probs_b, grad_out, preferred_element_type=jnp.float32)
    grad_rot = softmax_scale * jnp.einsum(
        "thk,thr->kr", grad_b, q_rot, preferred_element_type=jnp.float32
    )
    return grad_qlat, grad_qrot, jnp.concatenate([grad_lat, grad_rot], axis=1)


def local(q_latent, q_rope, attn_out, grad_out, log_total, latent, key_rope, doc_start):
    tok_rows, head_count, lat_width = q_latent.shape
    rope_width = key_rope.shape[1]
    span = 2**LEVELS
    half_span = span // 2
    groups = lax.axis_size("head")
    block = tok_rows // groups
    softmax_scale = (NOPE + ROPE) ** (-0.5)
    q_rot = q_rope.reshape(tok_rows, head_count, rope_width)
    row_delta = jnp.einsum("thc,thc->th", grad_out, attn_out, preferred_element_type=jnp.float32)
    own_tile = lax.axis_index("ctx")
    query_pos = own_tile * tok_rows + jnp.arange(tok_rows, dtype=jnp.int32)

    def terms(keys, first_tile):
        flat = keys.reshape(-1, lat_width + rope_width)
        return window_terms(
            q_latent, q_rot, grad_out, row_delta, log_total, doc_start, query_pos,
            flat, first_tile * tok_rows,
        )

    def group_sum(part):
        part = part.reshape(-1, groups, block, lat_width + rope_width)
        return lax.all_to_all(part, "head", 1, 1, tiled=True).sum(axis=1)

    near = jnp.concatenate([latent, key_rope], axis=1)[None]
    width = 1
    while width < half_span:
        near = jnp.concatenate([shifted(near, "ctx", width), near], axis=0)
        width *= 2
    far = shifted(near, "ctx", half_span)

    near_qlat, near_qrot, near_part = terms(near, own_tile - half_span + 1)
    far_qlat, far_qrot, far_part = terms(far, own_tile - span + 1)
    grad_qlat = softmax_scale * (near_qlat + far_qlat)
    grad_qrot = softmax_scale * (near_qrot + far_qrot)

    far_sum = shifted(group_sum(far_part), "ctx", -half_span)
    part = group_sum(near_part) + far_sum
    width = half_span
    while width > 1:
        half = width // 2
        part = part[half:] + shifted(part[:half], "ctx", -half)
        width = half
    owned = part[0]
    return (
        grad_qlat.astype(jnp.bfloat16),
        grad_qrot.reshape(tok_rows, head_count * rope_width).astype(jnp.bfloat16),
        owned[:, :lat_width].astype(jnp.bfloat16),
        owned[:, lat_width:].astype(jnp.bfloat16),
    )


def solution(mesh):
    in_specs = (
        P("ctx", "head", None),
        P("ctx", "head"),
        P("ctx", "head", None),
        P("ctx", "head", None),
        P("ctx", "head"),
        P("ctx", None),
        P("ctx", None),
        P("ctx"),
    )
    out_specs = (
        P("ctx", "head", None),
        P("ctx", "head"),
        P(("ctx", "head"), None),
        P(("ctx", "head"), None),
    )
    return jax.shard_map(local, mesh=mesh, in_specs=in_specs, out_specs=out_specs, check_vma=False)
```

```python
import jax
import jax.numpy as jnp
from jax import lax
from jax.sharding import PartitionSpec as P

ROPE = 64
NOPE = 128
LEVELS = 3


def shifted(x, axis, by):
    count = lax.axis_size(axis)
    pairs = [(i, i + by) for i in range(count) if 0 <= i + by < count]
    return lax.ppermute(x, axis, pairs)


def window_terms(q_latent, q_rot, grad_out, row_delta, log_total, doc_start, query_pos, keys, key_first):
    lat_width = q_latent.shape[2]
    softmax_scale = (NOPE + ROPE) ** (-0.5)
    lat_all = keys[:, :lat_width]
    rot_all = keys[:, lat_width:]
    key_pos = key_first + jnp.arange(keys.shape[0], dtype=jnp.int32)
    visible = (
        (key_pos[None, :] >= doc_start[:, None]) & (key_pos[None, :] <= query_pos[:, None])
    )[:, None, :]
    scores = (
        jnp.einsum("thc,kc->thk", q_latent, lat_all, preferred_element_type=jnp.float32)
        + jnp.einsum("thr,kr->thk", q_rot, rot_all, preferred_element_type=jnp.float32)
    ) * softmax_scale
    probs = jnp.where(
        visible, jnp.exp(jnp.where(visible, scores, 0.0) - log_total[:, :, None]), 0.0
    )
    grad_probs = jnp.einsum("thc,kc->thk", grad_out, lat_all, preferred_element_type=jnp.float32)
    grad_scores = probs * (grad_probs - row_delta[:, :, None])
    probs_b = probs.astype(jnp.bfloat16)
    grad_b = grad_scores.astype(jnp.bfloat16)
    grad_qlat = jnp.einsum("thk,kc->thc", grad_b, lat_all, preferred_element_type=jnp.float32)
    grad_qrot = jnp.einsum("thk,kr->thr", grad_b, rot_all, preferred_element_type=jnp.float32)
    grad_lat = softmax_scale * jnp.einsum(
        "thk,thc->kc", grad_b, q_latent, preferred_element_type=jnp.float32
    ) + jnp.einsum("thk,thc->kc", probs_b, grad_out, preferred_element_type=jnp.float32)
    grad_rot = softmax_scale * jnp.einsum(
        "thk,thr->kr", grad_b, q_rot, preferred_element_type=jnp.float32
    )
    return grad_qlat, grad_qrot, jnp.concatenate([grad_lat, grad_rot], axis=1)


def local(q_latent, q_rope, attn_out, grad_out, log_total, latent, key_rope, doc_start):
    tok_rows, head_count, lat_width = q_latent.shape
    rope_width = key_rope.shape[1]
    span = 2**LEVELS
    half_span = span // 2
    groups = lax.axis_size("head")
    block = tok_rows // groups
    softmax_scale = (NOPE + ROPE) ** (-0.5)
    q_rot = q_rope.reshape(tok_rows, head_count, rope_width)
    row_delta = jnp.einsum("thc,thc->th", grad_out, attn_out, preferred_element_type=jnp.float32)
    own_tile = lax.axis_index("ctx")
    query_pos = own_tile * tok_rows + jnp.arange(tok_rows, dtype=jnp.int32)

    def terms(keys, first_tile):
        flat = keys.reshape(-1, lat_width + rope_width)
        return window_terms(
            q_latent, q_rot, grad_out, row_delta, log_total, doc_start, query_pos,
            flat, first_tile * tok_rows,
        )

    def group_sum(part):
        part = part.reshape(-1, groups, block, lat_width + rope_width)
        return lax.all_to_all(part, "head", 1, 1, tiled=True).sum(axis=1)

    keys = jnp.concatenate([latent, key_rope], axis=1)
    rows = lax.dynamic_slice_in_dim(keys, lax.axis_index("head") * block, block, axis=0)[None]
    width = 1
    while width < half_span:
        rows = jnp.concatenate([shifted(rows, "ctx", width), rows], axis=0)
        width *= 2
    far_rows = shifted(rows, "ctx", half_span)

    def assemble(part):
        spread = jnp.broadcast_to(part[None], (groups,) + part.shape)
        got = lax.all_to_all(spread, "head", 0, 0, tiled=True)
        return got.transpose(1, 0, 2, 3)

    near = assemble(rows)
    far = assemble(far_rows)

    near_qlat, near_qrot, near_part = terms(near, own_tile - half_span + 1)
    far_qlat, far_qrot, far_part = terms(far, own_tile - span + 1)
    grad_qlat = softmax_scale * (near_qlat + far_qlat)
    grad_qrot = softmax_scale * (near_qrot + far_qrot)

    far_sum = shifted(group_sum(far_part), "ctx", -half_span)
    part = group_sum(near_part) + far_sum
    width = half_span
    while width > 1:
        half = width // 2
        part = part[half:] + shifted(part[:half], "ctx", -half)
        width = half
    owned = part[0]
    return (
        grad_qlat.astype(jnp.bfloat16),
        grad_qrot.reshape(tok_rows, head_count * rope_width).astype(jnp.bfloat16),
        owned[:, :lat_width].astype(jnp.bfloat16),
        owned[:, lat_width:].astype(jnp.bfloat16),
    )


def solution(mesh):
    in_specs = (
        P("ctx", "head", None),
        P("ctx", "head"),
        P("ctx", "head", None),
        P("ctx", "head", None),
        P("ctx", "head"),
        P("ctx", None),
        P("ctx", None),
        P("ctx"),
    )
    out_specs = (
        P("ctx", "head", None),
        P("ctx", "head"),
        P(("ctx", "head"), None),
        P(("ctx", "head"), None),
    )
    return jax.shard_map(local, mesh=mesh, in_specs=in_specs, out_specs=out_specs, check_vma=False)
```

```python
import jax
import jax.numpy as jnp
from jax import lax
from jax.sharding import PartitionSpec as P

ROPE = 64
NOPE = 128
LEVELS = 3


def shifted(x, axis, by):
    count = lax.axis_size(axis)
    pairs = [(i, i + by) for i in range(count) if 0 <= i + by < count]
    return lax.ppermute(x, axis, pairs)


def window_terms(q_latent, q_rot, grad_out, row_delta, log_total, doc_start, query_pos, keys, key_first):
    lat_width = q_latent.shape[2]
    softmax_scale = (NOPE + ROPE) ** (-0.5)
    lat_all = keys[:, :lat_width]
    rot_all = keys[:, lat_width:]
    key_pos = key_first + jnp.arange(keys.shape[0], dtype=jnp.int32)
    visible = (
        (key_pos[None, :] >= doc_start[:, None]) & (key_pos[None, :] <= query_pos[:, None])
    )[:, None, :]
    scores = (
        jnp.einsum("thc,kc->thk", q_latent, lat_all, preferred_element_type=jnp.float32)
        + jnp.einsum("thr,kr->thk", q_rot, rot_all, preferred_element_type=jnp.float32)
    ) * softmax_scale
    probs = jnp.where(
        visible, jnp.exp(jnp.where(visible, scores, 0.0) - log_total[:, :, None]), 0.0
    )
    grad_probs = jnp.einsum("thc,kc->thk", grad_out, lat_all, preferred_element_type=jnp.float32)
    grad_scores = probs * (grad_probs - row_delta[:, :, None])
    probs_b = probs.astype(jnp.bfloat16)
    grad_b = grad_scores.astype(jnp.bfloat16)
    grad_qlat = jnp.einsum("thk,kc->thc", grad_b, lat_all, preferred_element_type=jnp.float32)
    grad_qrot = jnp.einsum("thk,kr->thr", grad_b, rot_all, preferred_element_type=jnp.float32)
    grad_lat = softmax_scale * jnp.einsum(
        "thk,thc->kc", grad_b, q_latent, preferred_element_type=jnp.float32
    ) + jnp.einsum("thk,thc->kc", probs_b, grad_out, preferred_element_type=jnp.float32)
    grad_rot = softmax_scale * jnp.einsum(
        "thk,thr->kr", grad_b, q_rot, preferred_element_type=jnp.float32
    )
    return grad_qlat, grad_qrot, jnp.concatenate([grad_lat, grad_rot], axis=1)


def local(q_latent, q_rope, attn_out, grad_out, log_total, latent, key_rope, doc_start):
    tok_rows, head_count, lat_width = q_latent.shape
    rope_width = key_rope.shape[1]
    span = 2**LEVELS
    half_span = span // 2
    groups = lax.axis_size("head")
    block = tok_rows // groups
    softmax_scale = (NOPE + ROPE) ** (-0.5)
    q_rot = q_rope.reshape(tok_rows, head_count, rope_width)
    row_delta = jnp.einsum("thc,thc->th", grad_out, attn_out, preferred_element_type=jnp.float32)
    own_tile = lax.axis_index("ctx")
    query_pos = own_tile * tok_rows + jnp.arange(tok_rows, dtype=jnp.int32)

    def terms(keys, first_tile):
        flat = keys.reshape(-1, lat_width + rope_width)
        return window_terms(
            q_latent, q_rot, grad_out, row_delta, log_total, doc_start, query_pos,
            flat, first_tile * tok_rows,
        )

    def group_sum(part):
        part = part.reshape(-1, groups, block, lat_width + rope_width)
        part = part.astype(jnp.bfloat16)
        got = lax.all_to_all(part, "head", 1, 1, tiled=True)
        return got.astype(jnp.float32).sum(axis=1)

    keys = jnp.concatenate([latent, key_rope], axis=1)
    rows = lax.dynamic_slice_in_dim(keys, lax.axis_index("head") * block, block, axis=0)[None]
    width = 1
    while width < half_span:
        rows = jnp.concatenate([shifted(rows, "ctx", width), rows], axis=0)
        width *= 2
    far_rows = shifted(rows, "ctx", half_span)

    def assemble(part):
        spread = jnp.broadcast_to(part[None], (groups,) + part.shape)
        got = lax.all_to_all(spread, "head", 0, 0, tiled=True)
        return got.transpose(1, 0, 2, 3)

    near = assemble(rows)
    far = assemble(far_rows)

    near_qlat, near_qrot, near_part = terms(near, own_tile - half_span + 1)
    far_qlat, far_qrot, far_part = terms(far, own_tile - span + 1)
    grad_qlat = softmax_scale * (near_qlat + far_qlat)
    grad_qrot = softmax_scale * (near_qrot + far_qrot)

    far_sum = shifted(group_sum(far_part), "ctx", -half_span)
    part = group_sum(near_part) + far_sum
    width = half_span
    while width > 1:
        half = width // 2
        part = part[half:] + shifted(part[:half], "ctx", -half)
        width = half
    owned = part[0]
    return (
        grad_qlat.astype(jnp.bfloat16),
        grad_qrot.reshape(tok_rows, head_count * rope_width).astype(jnp.bfloat16),
        owned[:, :lat_width].astype(jnp.bfloat16),
        owned[:, lat_width:].astype(jnp.bfloat16),
    )


def solution(mesh):
    in_specs = (
        P("ctx", "head", None),
        P("ctx", "head"),
        P("ctx", "head", None),
        P("ctx", "head", None),
        P("ctx", "head"),
        P("ctx", None),
        P("ctx", None),
        P("ctx"),
    )
    out_specs = (
        P("ctx", "head", None),
        P("ctx", "head"),
        P(("ctx", "head"), None),
        P(("ctx", "head"), None),
    )
    return jax.shard_map(local, mesh=mesh, in_specs=in_specs, out_specs=out_specs, check_vma=False)
```

```python
import jax
import jax.numpy as jnp
from jax import lax
from jax.sharding import PartitionSpec as P

ROPE = 64
NOPE = 128
LEVELS = 3


def shifted(x, axis, by):
    count = lax.axis_size(axis)
    pairs = [(i, i + by) for i in range(count) if 0 <= i + by < count]
    return lax.ppermute(x, axis, pairs)


def window_terms(q_latent, q_rot, grad_out, row_delta, log_total, doc_start, query_pos, keys, key_first, key_order):
    lat_width = q_latent.shape[2]
    softmax_scale = (NOPE + ROPE) ** (-0.5)
    lat_all = keys[:, :lat_width]
    rot_all = keys[:, lat_width:]
    key_pos = key_first + key_order
    visible = (
        (key_pos[None, :] >= doc_start[:, None]) & (key_pos[None, :] <= query_pos[:, None])
    )[:, None, :]
    scores = (
        jnp.einsum("thc,kc->thk", q_latent, lat_all, preferred_element_type=jnp.float32)
        + jnp.einsum("thr,kr->thk", q_rot, rot_all, preferred_element_type=jnp.float32)
    ) * softmax_scale
    probs = jnp.where(
        visible, jnp.exp(jnp.where(visible, scores, 0.0) - log_total[:, :, None]), 0.0
    )
    grad_probs = jnp.einsum("thc,kc->thk", grad_out, lat_all, preferred_element_type=jnp.float32)
    grad_scores = probs * (grad_probs - row_delta[:, :, None])
    probs_b = probs.astype(jnp.bfloat16)
    grad_b = grad_scores.astype(jnp.bfloat16)
    grad_qlat = jnp.einsum("thk,kc->thc", grad_b, lat_all, preferred_element_type=jnp.float32)
    grad_qrot = jnp.einsum("thk,kr->thr", grad_b, rot_all, preferred_element_type=jnp.float32)
    grad_lat = softmax_scale * jnp.einsum(
        "thk,thc->kc", grad_b, q_latent, preferred_element_type=jnp.float32
    ) + jnp.einsum("thk,thc->kc", probs_b, grad_out, preferred_element_type=jnp.float32)
    grad_rot = softmax_scale * jnp.einsum(
        "thk,thr->kr", grad_b, q_rot, preferred_element_type=jnp.float32
    )
    return grad_qlat, grad_qrot, jnp.concatenate([grad_lat, grad_rot], axis=1)


def local(q_latent, q_rope, attn_out, grad_out, log_total, latent, key_rope, doc_start):
    tok_rows, head_count, lat_width = q_latent.shape
    rope_width = key_rope.shape[1]
    span = 2**LEVELS
    half_span = span // 2
    groups = lax.axis_size("head")
    block = tok_rows // groups
    softmax_scale = (NOPE + ROPE) ** (-0.5)
    q_rot = q_rope.reshape(tok_rows, head_count, rope_width)
    row_delta = jnp.einsum("thc,thc->th", grad_out, attn_out, preferred_element_type=jnp.float32)
    own_tile = lax.axis_index("ctx")
    query_pos = own_tile * tok_rows + jnp.arange(tok_rows, dtype=jnp.int32)

    key_order = (
        jnp.arange(groups, dtype=jnp.int32)[:, None, None] * block
        + jnp.arange(half_span, dtype=jnp.int32)[None, :, None] * tok_rows
        + jnp.arange(block, dtype=jnp.int32)[None, None, :]
    ).reshape(-1)

    def terms(keys, first_tile):
        flat = keys.reshape(-1, lat_width + rope_width)
        return window_terms(
            q_latent, q_rot, grad_out, row_delta, log_total, doc_start, query_pos,
            flat, first_tile * tok_rows, key_order,
        )

    def group_sum(part):
        part = part.reshape(groups, half_span, block, lat_width + rope_width)
        part = part.astype(jnp.bfloat16)
        got = lax.all_to_all(part, "head", 0, 0, tiled=True)
        return got.astype(jnp.float32).sum(axis=0)

    keys = jnp.concatenate([latent, key_rope], axis=1)
    rows = lax.dynamic_slice_in_dim(keys, lax.axis_index("head") * block, block, axis=0)[None]
    width = 1
    while width < half_span:
        rows = jnp.concatenate([shifted(rows, "ctx", width), rows], axis=0)
        width *= 2
    far_rows = shifted(rows, "ctx", half_span)

    def assemble(part):
        spread = jnp.broadcast_to(part[None], (groups,) + part.shape)
        return lax.all_to_all(spread, "head", 0, 0, tiled=True)

    near = assemble(rows)
    far = assemble(far_rows)

    near_qlat, near_qrot, near_part = terms(near, own_tile - half_span + 1)
    far_qlat, far_qrot, far_part = terms(far, own_tile - span + 1)
    grad_qlat = softmax_scale * (near_qlat + far_qlat)
    grad_qrot = softmax_scale * (near_qrot + far_qrot)

    far_sum = shifted(group_sum(far_part), "ctx", -half_span)
    part = group_sum(near_part) + far_sum
    width = half_span
    while width > 1:
        half = width // 2
        part = part[half:] + shifted(part[:half], "ctx", -half)
        width = half
    owned = part[0]
    return (
        grad_qlat.astype(jnp.bfloat16),
        grad_qrot.reshape(tok_rows, head_count * rope_width).astype(jnp.bfloat16),
        owned[:, :lat_width].astype(jnp.bfloat16),
        owned[:, lat_width:].astype(jnp.bfloat16),
    )


def solution(mesh):
    in_specs = (
        P("ctx", "head", None),
        P("ctx", "head"),
        P("ctx", "head", None),
        P("ctx", "head", None),
        P("ctx", "head"),
        P("ctx", None),
        P("ctx", None),
        P("ctx"),
    )
    out_specs = (
        P("ctx", "head", None),
        P("ctx", "head"),
        P(("ctx", "head"), None),
        P(("ctx", "head"), None),
    )
    return jax.shard_map(local, mesh=mesh, in_specs=in_specs, out_specs=out_specs, check_vma=False)
```

```python
import jax
import jax.numpy as jnp
from jax import lax
from jax.sharding import PartitionSpec as P

ROPE = 64
NOPE = 128
LEVELS = 3


def shifted(x, axis, by):
    count = lax.axis_size(axis)
    pairs = [(i, i + by) for i in range(count) if 0 <= i + by < count]
    return lax.ppermute(x, axis, pairs)


def window_terms(q_latent, q_rot, grad_out, row_delta, log_total, doc_start, query_pos, keys, key_first, key_order):
    lat_width = q_latent.shape[2]
    softmax_scale = (NOPE + ROPE) ** (-0.5)
    lat_all = keys[:, :lat_width]
    rot_all = keys[:, lat_width:]
    key_pos = key_first + key_order
    visible = (
        (key_pos[None, :] >= doc_start[:, None]) & (key_pos[None, :] <= query_pos[:, None])
    )[:, None, :]
    scores = (
        jnp.einsum("thc,kc->thk", q_latent, lat_all, preferred_element_type=jnp.float32)
        + jnp.einsum("thr,kr->thk", q_rot, rot_all, preferred_element_type=jnp.float32)
    ) * softmax_scale
    probs = jnp.where(
        visible, jnp.exp(jnp.where(visible, scores, 0.0) - log_total[:, :, None]), 0.0
    )
    grad_probs = jnp.einsum("thc,kc->thk", grad_out, lat_all, preferred_element_type=jnp.float32)
    grad_scores = probs * (grad_probs - row_delta[:, :, None])
    probs_b = probs.astype(jnp.bfloat16)
    grad_b = grad_scores.astype(jnp.bfloat16)
    grad_qlat = jnp.einsum("thk,kc->thc", grad_b, lat_all, preferred_element_type=jnp.float32)
    grad_qrot = jnp.einsum("thk,kr->thr", grad_b, rot_all, preferred_element_type=jnp.float32)
    grad_lat = softmax_scale * jnp.einsum(
        "thk,thc->kc", grad_b, q_latent, preferred_element_type=jnp.float32
    ) + jnp.einsum("thk,thc->kc", probs_b, grad_out, preferred_element_type=jnp.float32)
    grad_rot = softmax_scale * jnp.einsum(
        "thk,thr->kr", grad_b, q_rot, preferred_element_type=jnp.float32
    )
    return grad_qlat, grad_qrot, jnp.concatenate([grad_lat, grad_rot], axis=1)


def local(q_latent, q_rope, attn_out, grad_out, log_total, latent, key_rope, doc_start):
    tok_rows, head_count, lat_width = q_latent.shape
    rope_width = key_rope.shape[1]
    span = 2**LEVELS
    half_span = span // 2
    groups = lax.axis_size("head")
    block = tok_rows // groups
    softmax_scale = (NOPE + ROPE) ** (-0.5)
    q_rot = q_rope.reshape(tok_rows, head_count, rope_width)
    row_delta = jnp.einsum("thc,thc->th", grad_out, attn_out, preferred_element_type=jnp.float32)
    own_tile = lax.axis_index("ctx")
    query_pos = own_tile * tok_rows + jnp.arange(tok_rows, dtype=jnp.int32)

    key_order = (
        jnp.arange(groups, dtype=jnp.int32)[:, None, None] * block
        + jnp.arange(half_span, dtype=jnp.int32)[None, :, None] * tok_rows
        + jnp.arange(block, dtype=jnp.int32)[None, None, :]
    ).reshape(-1)

    def terms(keys, first_tile):
        flat = keys.reshape(-1, lat_width + rope_width)
        return window_terms(
            q_latent, q_rot, grad_out, row_delta, log_total, doc_start, query_pos,
            flat, first_tile * tok_rows, key_order,
        )

    def group_sum(part):
        part = part.reshape(groups, half_span, block, lat_width + rope_width)
        part = part.astype(jnp.bfloat16)
        got = lax.all_to_all(part, "head", 0, 0, tiled=True)
        return got.astype(jnp.float32).sum(axis=0)

    near_full = jnp.concatenate([latent, key_rope], axis=1)[None]
    width = 1
    while width < half_span:
        near_full = jnp.concatenate([shifted(near_full, "ctx", width), near_full], axis=0)
        width *= 2
    rows = lax.dynamic_slice_in_dim(near_full, lax.axis_index("head") * block, block, axis=1)
    far_rows = shifted(rows, "ctx", half_span)

    def assemble(part):
        spread = jnp.broadcast_to(part[None], (groups,) + part.shape)
        return lax.all_to_all(spread, "head", 0, 0, tiled=True)

    near = near_full.reshape(half_span, groups, block, -1).transpose(1, 0, 2, 3)
    far = assemble(far_rows)

    near_qlat, near_qrot, near_part = terms(near, own_tile - half_span + 1)
    far_qlat, far_qrot, far_part = terms(far, own_tile - span + 1)
    grad_qlat = softmax_scale * (near_qlat + far_qlat)
    grad_qrot = softmax_scale * (near_qrot + far_qrot)

    far_sum = shifted(group_sum(far_part), "ctx", -half_span)
    part = group_sum(near_part) + far_sum
    width = half_span
    while width > 1:
        half = width // 2
        part = part[half:] + shifted(part[:half], "ctx", -half)
        width = half
    owned = part[0]
    return (
        grad_qlat.astype(jnp.bfloat16),
        grad_qrot.reshape(tok_rows, head_count * rope_width).astype(jnp.bfloat16),
        owned[:, :lat_width].astype(jnp.bfloat16),
        owned[:, lat_width:].astype(jnp.bfloat16),
    )


def solution(mesh):
    in_specs = (
        P("ctx", "head", None),
        P("ctx", "head"),
        P("ctx", "head", None),
        P("ctx", "head", None),
        P("ctx", "head"),
        P("ctx", None),
        P("ctx", None),
        P("ctx"),
    )
    out_specs = (
        P("ctx", "head", None),
        P("ctx", "head"),
        P(("ctx", "head"), None),
        P(("ctx", "head"), None),
    )
    return jax.shard_map(local, mesh=mesh, in_specs=in_specs, out_specs=out_specs, check_vma=False)
```

```python
import jax
import jax.numpy as jnp
from jax import lax
from jax.sharding import PartitionSpec as P

ROPE = 64
NOPE = 128
LEVELS = 3


def shifted(x, axis, by):
    count = lax.axis_size(axis)
    pairs = [(i, i + by) for i in range(count) if 0 <= i + by < count]
    return lax.ppermute(x, axis, pairs)


def window_terms(q_latent, q_rot, grad_out, row_delta, log_total, doc_start, query_pos, keys, key_first, key_order):
    lat_width = q_latent.shape[2]
    softmax_scale = (NOPE + ROPE) ** (-0.5)
    lat_all = keys[:, :lat_width]
    rot_all = keys[:, lat_width:]
    key_pos = key_first + key_order
    visible = (
        (key_pos[None, :] >= doc_start[:, None]) & (key_pos[None, :] <= query_pos[:, None])
    )[:, None, :]
    scores = (
        jnp.einsum("thc,kc->thk", q_latent, lat_all, preferred_element_type=jnp.float32)
        + jnp.einsum("thr,kr->thk", q_rot, rot_all, preferred_element_type=jnp.float32)
    ) * softmax_scale
    probs = jnp.where(
        visible, jnp.exp(jnp.where(visible, scores, 0.0) - log_total[:, :, None]), 0.0
    )
    grad_probs = jnp.einsum("thc,kc->thk", grad_out, lat_all, preferred_element_type=jnp.float32)
    grad_scores = probs * (grad_probs - row_delta[:, :, None])
    probs_b = probs.astype(jnp.bfloat16)
    grad_b = grad_scores.astype(jnp.bfloat16)
    grad_qlat = jnp.einsum("thk,kc->thc", grad_b, lat_all, preferred_element_type=jnp.float32)
    grad_qrot = jnp.einsum("thk,kr->thr", grad_b, rot_all, preferred_element_type=jnp.float32)
    grad_lat = softmax_scale * jnp.einsum(
        "thk,thc->kc", grad_b, q_latent, preferred_element_type=jnp.float32
    ) + jnp.einsum("thk,thc->kc", probs_b, grad_out, preferred_element_type=jnp.float32)
    grad_rot = softmax_scale * jnp.einsum(
        "thk,thr->kr", grad_b, q_rot, preferred_element_type=jnp.float32
    )
    return grad_qlat, grad_qrot, jnp.concatenate([grad_lat, grad_rot], axis=1)


def local(q_latent, q_rope, attn_out, grad_out, log_total, latent, key_rope, doc_start):
    tok_rows, head_count, lat_width = q_latent.shape
    rope_width = key_rope.shape[1]
    span = 2**LEVELS
    half_span = span // 2
    groups = lax.axis_size("head")
    block = tok_rows // groups
    softmax_scale = (NOPE + ROPE) ** (-0.5)
    q_rot = q_rope.reshape(tok_rows, head_count, rope_width)
    row_delta = jnp.einsum("thc,thc->th", grad_out, attn_out, preferred_element_type=jnp.float32)
    own_tile = lax.axis_index("ctx")
    query_pos = own_tile * tok_rows + jnp.arange(tok_rows, dtype=jnp.int32)

    key_order = (
        jnp.arange(groups, dtype=jnp.int32)[:, None, None] * block
        + jnp.arange(half_span, dtype=jnp.int32)[None, :, None] * tok_rows
        + jnp.arange(block, dtype=jnp.int32)[None, None, :]
    ).reshape(-1)

    def terms(keys, first_tile):
        flat = keys.reshape(-1, lat_width + rope_width)
        return window_terms(
            q_latent, q_rot, grad_out, row_delta, log_total, doc_start, query_pos,
            flat, first_tile * tok_rows, key_order,
        )

    def group_sum(part):
        part = part.reshape(groups, half_span, block, lat_width + rope_width)
        part = part.astype(jnp.bfloat16)
        got = lax.all_to_all(part, "head", 0, 0, tiled=True)
        return got.astype(jnp.float32).sum(axis=0)

    near_full = jnp.concatenate([latent, key_rope], axis=1)[None]
    width = 1
    while width < half_span:
        near_full = jnp.concatenate([shifted(near_full, "ctx", width), near_full], axis=0)
        width *= 2
    rows = lax.dynamic_slice_in_dim(near_full, lax.axis_index("head") * block, block, axis=1)
    far_rows = shifted(rows, "ctx", half_span)

    def assemble(part):
        spread = jnp.broadcast_to(part[None], (groups,) + part.shape)
        return lax.all_to_all(spread, "head", 0, 0, tiled=True)

    near = near_full.reshape(half_span, groups, block, -1).transpose(1, 0, 2, 3)
    near_terms = terms(near, own_tile - half_span + 1)
    far_rows, near_terms = lax.optimization_barrier((far_rows, near_terms))
    near_qlat, near_qrot, near_part = near_terms
    far = assemble(far_rows)

    far_qlat, far_qrot, far_part = terms(far, own_tile - span + 1)
    grad_qlat = softmax_scale * (near_qlat + far_qlat)
    grad_qrot = softmax_scale * (near_qrot + far_qrot)

    far_sum = shifted(group_sum(far_part), "ctx", -half_span)
    part = group_sum(near_part) + far_sum
    width = half_span
    while width > 1:
        half = width // 2
        part = part[half:] + shifted(part[:half], "ctx", -half)
        width = half
    owned = part[0]
    return (
        grad_qlat.astype(jnp.bfloat16),
        grad_qrot.reshape(tok_rows, head_count * rope_width).astype(jnp.bfloat16),
        owned[:, :lat_width].astype(jnp.bfloat16),
        owned[:, lat_width:].astype(jnp.bfloat16),
    )


def solution(mesh):
    in_specs = (
        P("ctx", "head", None),
        P("ctx", "head"),
        P("ctx", "head", None),
        P("ctx", "head", None),
        P("ctx", "head"),
        P("ctx", None),
        P("ctx", None),
        P("ctx"),
    )
    out_specs = (
        P("ctx", "head", None),
        P("ctx", "head"),
        P(("ctx", "head"), None),
        P(("ctx", "head"), None),
    )
    return jax.shard_map(local, mesh=mesh, in_specs=in_specs, out_specs=out_specs, check_vma=False)
```

```python
import jax
import jax.numpy as jnp
from jax import lax
from jax.sharding import PartitionSpec as P

ROPE = 64
NOPE = 128
LEVELS = 3


def shifted(x, axis, by):
    count = lax.axis_size(axis)
    pairs = [(i, i + by) for i in range(count) if 0 <= i + by < count]
    return lax.ppermute(x, axis, pairs)


def window_terms(q_latent, q_rot, grad_out, row_delta, log_total, doc_start, query_pos, keys, key_first, key_order):
    lat_width = q_latent.shape[2]
    softmax_scale = (NOPE + ROPE) ** (-0.5)
    lat_all = keys[:, :lat_width]
    rot_all = keys[:, lat_width:]
    key_pos = key_first + key_order
    visible = (
        (key_pos[None, :] >= doc_start[:, None]) & (key_pos[None, :] <= query_pos[:, None])
    )[:, None, :]
    scores = (
        jnp.einsum("thc,kc->thk", q_latent, lat_all, preferred_element_type=jnp.float32)
        + jnp.einsum("thr,kr->thk", q_rot, rot_all, preferred_element_type=jnp.float32)
    ) * softmax_scale
    probs = jnp.where(
        visible, jnp.exp(jnp.where(visible, scores, 0.0) - log_total[:, :, None]), 0.0
    )
    grad_probs = jnp.einsum("thc,kc->thk", grad_out, lat_all, preferred_element_type=jnp.float32)
    grad_scores = probs * (grad_probs - row_delta[:, :, None])
    probs_b = probs.astype(jnp.bfloat16)
    grad_b = grad_scores.astype(jnp.bfloat16)
    grad_qlat = jnp.einsum("thk,kc->thc", grad_b, lat_all, preferred_element_type=jnp.float32)
    grad_qrot = jnp.einsum("thk,kr->thr", grad_b, rot_all, preferred_element_type=jnp.float32)
    grad_lat = softmax_scale * jnp.einsum(
        "thk,thc->kc", grad_b, q_latent, preferred_element_type=jnp.float32
    ) + jnp.einsum("thk,thc->kc", probs_b, grad_out, preferred_element_type=jnp.float32)
    grad_rot = softmax_scale * jnp.einsum(
        "thk,thr->kr", grad_b, q_rot, preferred_element_type=jnp.float32
    )
    return grad_qlat, grad_qrot, jnp.concatenate([grad_lat, grad_rot], axis=1)


def local(q_latent, q_rope, attn_out, grad_out, log_total, latent, key_rope, doc_start):
    tok_rows, head_count, lat_width = q_latent.shape
    rope_width = key_rope.shape[1]
    span = 2**LEVELS
    half_span = span // 2
    groups = lax.axis_size("head")
    block = tok_rows // groups
    softmax_scale = (NOPE + ROPE) ** (-0.5)
    q_rot = q_rope.reshape(tok_rows, head_count, rope_width)
    row_delta = jnp.einsum("thc,thc->th", grad_out, attn_out, preferred_element_type=jnp.float32)
    own_tile = lax.axis_index("ctx")
    query_pos = own_tile * tok_rows + jnp.arange(tok_rows, dtype=jnp.int32)

    key_order = (
        jnp.arange(groups, dtype=jnp.int32)[:, None, None] * block
        + jnp.arange(half_span, dtype=jnp.int32)[None, :, None] * tok_rows
        + jnp.arange(block, dtype=jnp.int32)[None, None, :]
    ).reshape(-1)

    def terms(keys, first_tile):
        flat = keys.reshape(-1, lat_width + rope_width)
        return window_terms(
            q_latent, q_rot, grad_out, row_delta, log_total, doc_start, query_pos,
            flat, first_tile * tok_rows, key_order,
        )

    def group_sum(part):
        part = part.reshape(groups, half_span, block, lat_width + rope_width)
        part = part.astype(jnp.bfloat16)
        got = lax.all_to_all(part, "head", 0, 0, tiled=True)
        return got.astype(jnp.float32).sum(axis=0)

    pair = jnp.concatenate([latent, key_rope], axis=1)[None]
    pair = jnp.concatenate([shifted(pair, "ctx", 1), pair], axis=0)
    near_full = jnp.concatenate([shifted(pair, "ctx", 2), pair], axis=0)
    rows = lax.dynamic_slice_in_dim(pair, lax.axis_index("head") * block, block, axis=1)
    far_rows = jnp.concatenate(
        [shifted(rows, "ctx", half_span + 2), shifted(rows, "ctx", half_span)], axis=0
    )

    def assemble(part):
        spread = jnp.broadcast_to(part[None], (groups,) + part.shape)
        return lax.all_to_all(spread, "head", 0, 0, tiled=True)

    near = near_full.reshape(half_span, groups, block, -1).transpose(1, 0, 2, 3)
    far = assemble(far_rows)

    near_qlat, near_qrot, near_part = terms(near, own_tile - half_span + 1)
    far_qlat, far_qrot, far_part = terms(far, own_tile - span + 1)
    grad_qlat = softmax_scale * (near_qlat + far_qlat)
    grad_qrot = softmax_scale * (near_qrot + far_qrot)

    far_sum = shifted(group_sum(far_part), "ctx", -half_span)
    part = group_sum(near_part) + far_sum
    width = half_span
    while width > 1:
        half = width // 2
        part = part[half:] + shifted(part[:half], "ctx", -half)
        width = half
    owned = part[0]
    return (
        grad_qlat.astype(jnp.bfloat16),
        grad_qrot.reshape(tok_rows, head_count * rope_width).astype(jnp.bfloat16),
        owned[:, :lat_width].astype(jnp.bfloat16),
        owned[:, lat_width:].astype(jnp.bfloat16),
    )


def solution(mesh):
    in_specs = (
        P("ctx", "head", None),
        P("ctx", "head"),
        P("ctx", "head", None),
        P("ctx", "head", None),
        P("ctx", "head"),
        P("ctx", None),
        P("ctx", None),
        P("ctx"),
    )
    out_specs = (
        P("ctx", "head", None),
        P("ctx", "head"),
        P(("ctx", "head"), None),
        P(("ctx", "head"), None),
    )
    return jax.shard_map(local, mesh=mesh, in_specs=in_specs, out_specs=out_specs, check_vma=False)
```

```python
import jax
import jax.numpy as jnp
from jax import lax
from jax.sharding import PartitionSpec as P

ROPE = 64
NOPE = 128
LEVELS = 3


def shifted(x, axis, by):
    count = lax.axis_size(axis)
    pairs = [(i, i + by) for i in range(count) if 0 <= i + by < count]
    return lax.ppermute(x, axis, pairs)


def window_terms(q_latent, q_rot, grad_out, row_delta, log_total, doc_start, query_pos, keys, key_first, key_order):
    lat_width = q_latent.shape[2]
    softmax_scale = (NOPE + ROPE) ** (-0.5)
    lat_all = keys[:, :lat_width]
    rot_all = keys[:, lat_width:]
    key_pos = key_first + key_order
    visible = (
        (key_pos[None, :] >= doc_start[:, None]) & (key_pos[None, :] <= query_pos[:, None])
    )[:, None, :]
    scores = (
        jnp.einsum("thc,kc->thk", q_latent, lat_all, preferred_element_type=jnp.float32)
        + jnp.einsum("thr,kr->thk", q_rot, rot_all, preferred_element_type=jnp.float32)
    ) * softmax_scale
    probs = jnp.where(
        visible, jnp.exp(jnp.where(visible, scores, 0.0) - log_total[:, :, None]), 0.0
    )
    grad_probs = jnp.einsum("thc,kc->thk", grad_out, lat_all, preferred_element_type=jnp.float32)
    grad_scores = probs * (grad_probs - row_delta[:, :, None])
    probs_b = probs.astype(jnp.bfloat16)
    grad_b = grad_scores.astype(jnp.bfloat16)
    grad_qlat = jnp.einsum("thk,kc->thc", grad_b, lat_all, preferred_element_type=jnp.float32)
    grad_qrot = jnp.einsum("thk,kr->thr", grad_b, rot_all, preferred_element_type=jnp.float32)
    grad_lat = softmax_scale * jnp.einsum(
        "thk,thc->kc", grad_b, q_latent, preferred_element_type=jnp.float32
    ) + jnp.einsum("thk,thc->kc", probs_b, grad_out, preferred_element_type=jnp.float32)
    grad_rot = softmax_scale * jnp.einsum(
        "thk,thr->kr", grad_b, q_rot, preferred_element_type=jnp.float32
    )
    return grad_qlat, grad_qrot, jnp.concatenate([grad_lat, grad_rot], axis=1)


def local(q_latent, q_rope, attn_out, grad_out, log_total, latent, key_rope, doc_start):
    tok_rows, head_count, lat_width = q_latent.shape
    rope_width = key_rope.shape[1]
    span = 2**LEVELS
    half_span = span // 2
    groups = lax.axis_size("head")
    block = tok_rows // groups
    softmax_scale = (NOPE + ROPE) ** (-0.5)
    q_rot = q_rope.reshape(tok_rows, head_count, rope_width)
    row_delta = jnp.einsum("thc,thc->th", grad_out, attn_out, preferred_element_type=jnp.float32)
    own_tile = lax.axis_index("ctx")
    query_pos = own_tile * tok_rows + jnp.arange(tok_rows, dtype=jnp.int32)

    key_order = (
        jnp.arange(groups, dtype=jnp.int32)[:, None, None] * block
        + jnp.arange(half_span, dtype=jnp.int32)[None, :, None] * tok_rows
        + jnp.arange(block, dtype=jnp.int32)[None, None, :]
    ).reshape(-1)

    def terms(keys, first_tile):
        flat = keys.reshape(-1, lat_width + rope_width)
        return window_terms(
            q_latent, q_rot, grad_out, row_delta, log_total, doc_start, query_pos,
            flat, first_tile * tok_rows, key_order,
        )

    def group_sum(part):
        part = part.reshape(groups, half_span, block, lat_width + rope_width)
        part = part.astype(jnp.bfloat16)
        got = lax.all_to_all(part, "head", 0, 0, tiled=True)
        return got.astype(jnp.float32).sum(axis=0)

    pair = jnp.concatenate([latent, key_rope], axis=1)[None]
    pair = jnp.concatenate([shifted(pair, "ctx", 1), pair], axis=0)
    near_full = jnp.concatenate([shifted(pair, "ctx", 2), pair], axis=0)
    rows = lax.dynamic_slice_in_dim(pair, lax.axis_index("head") * block, block, axis=1)
    far_rows = jnp.concatenate(
        [shifted(rows, "ctx", half_span + 2), shifted(rows, "ctx", half_span)], axis=0
    )

    def assemble(part):
        spread = jnp.broadcast_to(part[None], (groups,) + part.shape)
        return lax.all_to_all(spread, "head", 0, 0, tiled=True)

    near = near_full.reshape(half_span, groups, block, -1).transpose(1, 0, 2, 3)
    far = assemble(far_rows)

    near_qlat, near_qrot, near_part = terms(near, own_tile - half_span + 1)
    far_qlat, far_qrot, far_part = terms(far, own_tile - span + 1)
    grad_qlat = softmax_scale * (near_qlat + far_qlat)
    grad_qrot = softmax_scale * (near_qrot + far_qrot)

    part = jnp.concatenate(
        [
            far_part.reshape(groups, half_span, block, lat_width + rope_width),
            near_part.reshape(groups, half_span, block, lat_width + rope_width),
        ],
        axis=1,
    ).astype(jnp.bfloat16)
    part = lax.all_to_all(part, "head", 0, 0, tiled=True).astype(jnp.float32).sum(axis=0)
    width = span
    while width > 1:
        half = width // 2
        part = part[half:] + shifted(part[:half], "ctx", -half)
        width = half
    owned = part[0]
    return (
        grad_qlat.astype(jnp.bfloat16),
        grad_qrot.reshape(tok_rows, head_count * rope_width).astype(jnp.bfloat16),
        owned[:, :lat_width].astype(jnp.bfloat16),
        owned[:, lat_width:].astype(jnp.bfloat16),
    )


def solution(mesh):
    in_specs = (
        P("ctx", "head", None),
        P("ctx", "head"),
        P("ctx", "head", None),
        P("ctx", "head", None),
        P("ctx", "head"),
        P("ctx", None),
        P("ctx", None),
        P("ctx"),
    )
    out_specs = (
        P("ctx", "head", None),
        P("ctx", "head"),
        P(("ctx", "head"), None),
        P(("ctx", "head"), None),
    )
    return jax.shard_map(local, mesh=mesh, in_specs=in_specs, out_specs=out_specs, check_vma=False)
```

```python
import jax
import jax.numpy as jnp
from jax import lax
from jax.sharding import PartitionSpec as P

ROPE = 64
NOPE = 128
LEVELS = 3


def shifted(x, axis, by):
    count = lax.axis_size(axis)
    pairs = [(i, i + by) for i in range(count) if 0 <= i + by < count]
    return lax.ppermute(x, axis, pairs)


def window_terms(q_latent, q_rot, grad_out, row_delta, log_total, doc_start, query_pos, keys, key_first, key_order):
    lat_width = q_latent.shape[2]
    softmax_scale = (NOPE + ROPE) ** (-0.5)
    lat_all = keys[:, :lat_width]
    rot_all = keys[:, lat_width:]
    key_pos = key_first + key_order
    visible = (
        (key_pos[None, :] >= doc_start[:, None]) & (key_pos[None, :] <= query_pos[:, None])
    )[:, None, :]
    scores = (
        jnp.einsum("thc,kc->thk", q_latent, lat_all, preferred_element_type=jnp.float32)
        + jnp.einsum("thr,kr->thk", q_rot, rot_all, preferred_element_type=jnp.float32)
    ) * softmax_scale
    probs = jnp.where(
        visible, jnp.exp(jnp.where(visible, scores, 0.0) - log_total[:, :, None]), 0.0
    )
    grad_probs = jnp.einsum("thc,kc->thk", grad_out, lat_all, preferred_element_type=jnp.float32)
    grad_scores = probs * (grad_probs - row_delta[:, :, None])
    probs_b = probs.astype(jnp.bfloat16)
    grad_b = grad_scores.astype(jnp.bfloat16)
    grad_qlat = jnp.einsum("thk,kc->thc", grad_b, lat_all, preferred_element_type=jnp.float32)
    grad_qrot = jnp.einsum("thk,kr->thr", grad_b, rot_all, preferred_element_type=jnp.float32)
    grad_lat = softmax_scale * jnp.einsum(
        "thk,thc->kc", grad_b, q_latent, preferred_element_type=jnp.float32
    ) + jnp.einsum("thk,thc->kc", probs_b, grad_out, preferred_element_type=jnp.float32)
    grad_rot = softmax_scale * jnp.einsum(
        "thk,thr->kr", grad_b, q_rot, preferred_element_type=jnp.float32
    )
    return grad_qlat, grad_qrot, jnp.concatenate([grad_lat, grad_rot], axis=1)


def local(q_latent, q_rope, attn_out, grad_out, log_total, latent, key_rope, doc_start):
    tok_rows, head_count, lat_width = q_latent.shape
    rope_width = key_rope.shape[1]
    span = 2**LEVELS
    half_span = span // 2
    groups = lax.axis_size("head")
    block = tok_rows // groups
    softmax_scale = (NOPE + ROPE) ** (-0.5)
    q_rot = q_rope.reshape(tok_rows, head_count, rope_width)
    row_delta = jnp.einsum("thc,thc->th", grad_out, attn_out, preferred_element_type=jnp.float32)
    own_tile = lax.axis_index("ctx")
    query_pos = own_tile * tok_rows + jnp.arange(tok_rows, dtype=jnp.int32)

    key_order = (
        jnp.arange(groups, dtype=jnp.int32)[:, None, None] * block
        + jnp.arange(half_span, dtype=jnp.int32)[None, :, None] * tok_rows
        + jnp.arange(block, dtype=jnp.int32)[None, None, :]
    ).reshape(-1)

    def terms(keys, first_tile):
        flat = keys.reshape(-1, lat_width + rope_width)
        return window_terms(
            q_latent, q_rot, grad_out, row_delta, log_total, doc_start, query_pos,
            flat, first_tile * tok_rows, key_order,
        )

    def group_sum(part):
        part = part.reshape(groups, half_span, block, lat_width + rope_width)
        part = part.astype(jnp.bfloat16)
        got = lax.all_to_all(part, "head", 0, 0, tiled=True)
        return got.astype(jnp.float32).sum(axis=0)

    pair = jnp.concatenate([latent, key_rope], axis=1)[None]
    pair = jnp.concatenate([shifted(pair, "ctx", 1), pair], axis=0)
    near_full = jnp.concatenate([shifted(pair, "ctx", 2), pair], axis=0)
    rows = lax.dynamic_slice_in_dim(pair, lax.axis_index("head") * block, block, axis=1)
    far_rows = jnp.concatenate(
        [shifted(rows, "ctx", half_span + 2), shifted(rows, "ctx", half_span)], axis=0
    )

    def assemble(part):
        spread = jnp.broadcast_to(part[None], (groups,) + part.shape)
        return lax.all_to_all(spread, "head", 0, 0, tiled=True)

    near = near_full.reshape(half_span, groups, block, -1).transpose(1, 0, 2, 3)
    far = assemble(far_rows)

    near_qlat, near_qrot, near_part = terms(near, own_tile - half_span + 1)
    far_qlat, far_qrot, far_part = terms(far, own_tile - span + 1)
    grad_qlat = softmax_scale * (near_qlat + far_qlat)
    grad_qrot = softmax_scale * (near_qrot + far_qrot)

    far_sum = group_sum(far_part)
    near_part, far_sum = lax.optimization_barrier((near_part, far_sum))
    far_sum = shifted(far_sum, "ctx", -half_span)
    part = group_sum(near_part) + far_sum
    width = half_span
    while width > 2:
        half = width // 2
        part = part[half:] + shifted(part[:half], "ctx", -half)
        width = half
    last = shifted(part[0], "ctx", -1)
    return (
        grad_qlat.astype(jnp.bfloat16),
        grad_qrot.reshape(tok_rows, head_count * rope_width).astype(jnp.bfloat16),
        (part[1, :, :lat_width] + last[:, :lat_width]).astype(jnp.bfloat16),
        (part[1, :, lat_width:] + last[:, lat_width:]).astype(jnp.bfloat16),
    )


def solution(mesh):
    in_specs = (
        P("ctx", "head", None),
        P("ctx", "head"),
        P("ctx", "head", None),
        P("ctx", "head", None),
        P("ctx", "head"),
        P("ctx", None),
        P("ctx", None),
        P("ctx"),
    )
    out_specs = (
        P("ctx", "head", None),
        P("ctx", "head"),
        P(("ctx", "head"), None),
        P(("ctx", "head"), None),
    )
    return jax.shard_map(local, mesh=mesh, in_specs=in_specs, out_specs=out_specs, check_vma=False)
```

```python
import jax
import jax.numpy as jnp
from jax import lax
from jax.sharding import PartitionSpec as P

ROPE = 64
NOPE = 128
LEVELS = 3


def shifted(x, axis, by):
    count = lax.axis_size(axis)
    pairs = [(i, i + by) for i in range(count) if 0 <= i + by < count]
    return lax.ppermute(x, axis, pairs)


def window_terms(q_latent, q_rot, grad_out, row_delta, log_total, doc_start, query_pos, keys, key_first, key_order):
    lat_width = q_latent.shape[2]
    softmax_scale = (NOPE + ROPE) ** (-0.5)
    lat_all = keys[:, :lat_width]
    rot_all = keys[:, lat_width:]
    key_pos = key_first + key_order
    visible = (
        (key_pos[None, :] >= doc_start[:, None]) & (key_pos[None, :] <= query_pos[:, None])
    )[:, None, :]
    scores = (
        jnp.einsum("thc,kc->thk", q_latent, lat_all, preferred_element_type=jnp.float32)
        + jnp.einsum("thr,kr->thk", q_rot, rot_all, preferred_element_type=jnp.float32)
    ) * softmax_scale
    probs = jnp.where(
        visible, jnp.exp(jnp.where(visible, scores, 0.0) - log_total[:, :, None]), 0.0
    )
    grad_probs = jnp.einsum("thc,kc->thk", grad_out, lat_all, preferred_element_type=jnp.float32)
    grad_scores = probs * (grad_probs - row_delta[:, :, None])
    probs_b = probs.astype(jnp.bfloat16)
    grad_b = grad_scores.astype(jnp.bfloat16)
    grad_qlat = jnp.einsum("thk,kc->thc", grad_b, lat_all, preferred_element_type=jnp.float32)
    grad_qrot = jnp.einsum("thk,kr->thr", grad_b, rot_all, preferred_element_type=jnp.float32)
    grad_lat = softmax_scale * jnp.einsum(
        "thk,thc->kc", grad_b, q_latent, preferred_element_type=jnp.float32
    ) + jnp.einsum("thk,thc->kc", probs_b, grad_out, preferred_element_type=jnp.float32)
    grad_rot = softmax_scale * jnp.einsum(
        "thk,thr->kr", grad_b, q_rot, preferred_element_type=jnp.float32
    )
    return grad_qlat, grad_qrot, jnp.concatenate([grad_lat, grad_rot], axis=1)


def local(q_latent, q_rope, attn_out, grad_out, log_total, latent, key_rope, doc_start):
    tok_rows, head_count, lat_width = q_latent.shape
    rope_width = key_rope.shape[1]
    span = 2**LEVELS
    half_span = span // 2
    groups = lax.axis_size("head")
    block = tok_rows // groups
    softmax_scale = (NOPE + ROPE) ** (-0.5)
    q_rot = q_rope.reshape(tok_rows, head_count, rope_width)
    row_delta = jnp.einsum("thc,thc->th", grad_out, attn_out, preferred_element_type=jnp.float32)
    own_tile = lax.axis_index("ctx")
    query_pos = own_tile * tok_rows + jnp.arange(tok_rows, dtype=jnp.int32)

    key_order = (
        jnp.arange(groups, dtype=jnp.int32)[:, None, None] * block
        + jnp.arange(half_span, dtype=jnp.int32)[None, :, None] * tok_rows
        + jnp.arange(block, dtype=jnp.int32)[None, None, :]
    ).reshape(-1)

    def terms(keys, first_tile):
        flat = keys.reshape(-1, lat_width + rope_width)
        return window_terms(
            q_latent, q_rot, grad_out, row_delta, log_total, doc_start, query_pos,
            flat, first_tile * tok_rows, key_order,
        )

    def group_sum(part):
        part = part.reshape(groups, half_span, block, lat_width + rope_width)
        part = part.astype(jnp.bfloat16)
        got = lax.all_to_all(part, "head", 0, 0, tiled=True)
        return got.astype(jnp.float32).sum(axis=0)

    pair = jnp.concatenate([latent, key_rope], axis=1)[None]
    pair = jnp.concatenate([shifted(pair, "ctx", 1), pair], axis=0)
    near_full = jnp.concatenate([shifted(pair, "ctx", 2), pair], axis=0)
    rows = lax.dynamic_slice_in_dim(pair, lax.axis_index("head") * block, block, axis=1)
    far_rows = jnp.concatenate(
        [shifted(rows, "ctx", half_span + 2), shifted(rows, "ctx", half_span)], axis=0
    )

    def assemble(part):
        spread = jnp.broadcast_to(part[None], (groups,) + part.shape)
        return lax.all_to_all(spread, "head", 0, 0, tiled=True)

    near = near_full.reshape(half_span, groups, block, -1).transpose(1, 0, 2, 3)
    far = assemble(far_rows)

    near_qlat, near_qrot, near_part = terms(near, own_tile - half_span + 1)
    far_qlat, far_qrot, far_part = terms(far, own_tile - span + 1)
    grad_qlat = softmax_scale * (near_qlat + far_qlat)
    grad_qrot = softmax_scale * (near_qrot + far_qrot)

    far_sum = shifted(group_sum(far_part), "ctx", -half_span)
    part = group_sum(near_part) + far_sum
    width = half_span
    while width > 2:
        half = width // 2
        part = part[half:] + shifted(part[:half], "ctx", -half)
        width = half
    last = shifted(part[0], "ctx", -1)
    return (
        grad_qlat.astype(jnp.bfloat16),
        grad_qrot.reshape(tok_rows, head_count * rope_width).astype(jnp.bfloat16),
        (part[1, :, :lat_width] + last[:, :lat_width]).astype(jnp.bfloat16),
        (part[1, :, lat_width:] + last[:, lat_width:]).astype(jnp.bfloat16),
    )


def solution(mesh):
    in_specs = (
        P("ctx", "head", None),
        P("ctx", "head"),
        P("ctx", "head", None),
        P("ctx", "head", None),
        P("ctx", "head"),
        P("ctx", None),
        P("ctx", None),
        P("ctx"),
    )
    out_specs = (
        P("ctx", "head", None),
        P("ctx", "head"),
        P(("ctx", "head"), None),
        P(("ctx", "head"), None),
    )
    return jax.shard_map(local, mesh=mesh, in_specs=in_specs, out_specs=out_specs, check_vma=False)
```
